1024 devices in a mesh: dom: 2 (over core), gx: 32 (over z_hi, y, x), gy: 16 (over z_lo).
Axes of the slice: x: 4, y: 4, z: 32 (z_hi: 2, z_lo: 16; z = z_hi * 16 + z_lo), core: 2. Of those that a mesh axis runs over, the one named last changes fastest.
Arguments:
- velocity: float32 [2, 3, 512, 128, 128], P('dom', None, 'gx', 'gy'), may hold values from -5 to 5
- fringe_start: int32 [1], replicated, may hold values from 0 to 511
Outputs:
- velocity_out: float32 [2, 3, 512, 128, 128], P('dom', None, 'gx', 'gy')
- spectrum: float32 [2, 128, 512, 128], P(None, ('dom', 'gx'), 'gy')
The draws below stay inside these ranges and needn't reach their ends.
All inputs are finite; a program needn't handle non-finite values.
Results may differ from the reference program's by a relative error of at most 0.000084.
Values sent between devices are 32-bit elements; how exact they have to be, the bound alone decides.
No kernel may reach another device: no remote copies, remote signals or barrier semaphores. Data moves between devices by JAX's collectives and lax.ppermute only.
A program may use at most 32 MiB of HBM per device.

```python
import math
import jax
import jax.numpy as jnp

NZ = 128
NX = 512
NY = 128
FRINGE = 128


def steps_of(stream_key, dims, cuts, low, top_value):
    gain, own = 1.0, jax.random.fold_in(stream_key, 6)
    for dim, blocks in cuts:
        draws = jnp.exp(jax.random.uniform(jax.random.fold_in(own, dim), (blocks,), jnp.float32, low / len(cuts), top_value / len(cuts)))
        gain = gain * jnp.repeat(draws, dims[dim] // blocks).reshape([-1 if axis == dim else 1 for axis in range(len(dims))])
    return gain


def normal_values(key, dims, deviation, most, pieces=(), held_as=jnp.bfloat16):
    factor_of = steps_of(key, dims, pieces, -0.22, 0.18) if pieces else 1.0
    result = jax.random.normal(key, dims, jnp.float32) * deviation * factor_of
    return jnp.minimum(jnp.maximum(result, -most), most).astype(held_as)


def setup_inputs(seed: int = 0) -> dict:
    arg_keys = jax.random.split(jax.random.key(seed), 3)
    return {
        "velocity": normal_values(arg_keys[0], (2, 3, NX, NY, NZ), 1.0, 5.0, ((0, 2), (2, 32), (3, 16)), jnp.float32),
        "fringe_start": jax.random.randint(arg_keys[1], (1,), 0, NX).astype(jnp.int32),
    }


time_step = 0.1
fringe_rate = 1.0
smag_coef = 0.03
base_visc = 0.02
strain_floor = 0.25

def combine(center, x_plus, x_minus, y_plus, y_minus, z_plus, z_minus, inflow, fringe_ramp):
    grad_x = 0.5 * (x_plus - x_minus)
    grad_y = 0.5 * (y_plus - y_minus)
    grad_z = 0.5 * (z_plus - z_minus)
    gradients = (grad_x, grad_y, grad_z)
    strain = jnp.zeros_like(center[0])
    for comp_a in range(3):
        for comp_b in range(3):
            sym_part = 0.5 * (gradients[comp_b][comp_a] + gradients[comp_a][comp_b])
            strain = strain + sym_part * sym_part
    eddy_visc = base_visc + smag_coef * jnp.sqrt(2.0 * strain + strain_floor)
    advection = center[0] * grad_x + center[1] * grad_y + center[2] * grad_z
    laplace_term = x_plus + x_minus + y_plus + y_minus + z_plus + z_minus - 6.0 * center
    return -advection + eddy_visc * laplace_term + fringe_ramp * (inflow - center)

def ramp_values(fringe_start, x_cells, fringe_len, total_len):
    offset = (x_cells - fringe_start[0] + total_len) % total_len
    inside = offset < fringe_len
    sine_part = jnp.sin((offset.astype(jnp.float32) + 0.5) * (math.pi / fringe_len))
    return jnp.where(inside, fringe_rate * sine_part * sine_part, 0.0)

def periodic_tendency(field, inflow, fringe_ramp):
    padded = jnp.pad(field, ((0, 0), (0, 0), (0, 0), (1, 1)))
    return combine(field, jnp.roll(field, -1, 1), jnp.roll(field, 1, 1), jnp.roll(field, -1, 2), jnp.roll(field, 1, 2), padded[..., 2:], padded[..., :-2], inflow, fringe_ramp)

def reference(velocity, fringe_start):
    x_cells = jnp.arange(NX, dtype=jnp.int32)
    fringe_ramp = ramp_values(fringe_start, x_cells, FRINGE, NX).reshape(NX, 1, 1)
    inflow = velocity[0]
    results = []
    for domain in range(2):
        start_field = velocity[domain]
        ramp_here = fringe_ramp * float(domain)
        section_one = start_field + time_step * periodic_tendency(start_field, inflow, ramp_here)
        section_two = 0.75 * start_field + 0.25 * (section_one + time_step * periodic_tendency(section_one, inflow, ramp_here))
        section_three = 1.0 / 3.0 * start_field + 2.0 / 3.0 * (section_two + time_step * periodic_tendency(section_two, inflow, ramp_here))
        results.append(section_three)
    farm_field = results[1]
    padded = jnp.pad(farm_field[2], ((0, 0), (0, 0), (1, 1)))
    divergence = 0.5 * (jnp.roll(farm_field[0], -1, 0) - jnp.roll(farm_field[0], 1, 0)) + 0.5 * (jnp.roll(farm_field[1], -1, 1) - jnp.roll(farm_field[1], 1, 1)) + 0.5 * (padded[:, :, 2:] - padded[:, :, :-2])
    transform = jnp.fft.fft2(divergence, axes=(0, 1), norm='ortho')
    transform = jnp.transpose(transform, (2, 0, 1))
    spectrum = jnp.stack([jnp.real(transform), jnp.imag(transform)]).astype(jnp.float32)
    return (jnp.stack(results), spectrum)
```

```python
import math

import jax
import jax.numpy as jnp
from jax import lax
from jax.sharding import PartitionSpec as P

time_step = 0.1
fringe_rate = 1.0
smag_coef = 0.03
base_visc = 0.02
strain_floor = 0.25

HALO = 4


def shift_pairs(count_x, count_y, step_x, step_y):
    pairs = []
    for gx in range(count_x):
        for gy in range(count_y):
            source = gx * count_y + gy
            target = ((gx + step_x) % count_x) * count_y + (gy + step_y) % count_y
            pairs.append((source, target))
    return pairs


def with_halo_2d(block, width):
    count_x = lax.axis_size("gx")
    count_y = lax.axis_size("gy")
    axes = ("gx", "gy")

    def send(piece, step_x, step_y):
        return lax.ppermute(piece, axes, shift_pairs(count_x, count_y, step_x, step_y))

    lo_x = slice(0, width)
    hi_x = slice(block.shape[1] - width, None)
    lo_y = slice(0, width)
    hi_y = slice(block.shape[2] - width, None)
    every = slice(None)
    from_xm = send(block[:, hi_x, every], 1, 0)
    from_xp = send(block[:, lo_x, every], -1, 0)
    from_ym = send(block[:, every, hi_y], 0, 1)
    from_yp = send(block[:, every, lo_y], 0, -1)
    from_xm_ym = send(block[:, hi_x, hi_y], 1, 1)
    from_xm_yp = send(block[:, hi_x, lo_y], 1, -1)
    from_xp_ym = send(block[:, lo_x, hi_y], -1, 1)
    from_xp_yp = send(block[:, lo_x, lo_y], -1, -1)
    low = jnp.concatenate([from_xm_ym, from_xm, from_xm_yp], axis=2)
    mid = jnp.concatenate([from_ym, block, from_yp], axis=2)
    high = jnp.concatenate([from_xp_ym, from_xp, from_xp_yp], axis=2)
    return jnp.concatenate([low, mid, high], axis=1)


def combine(center, x_plus, x_minus, y_plus, y_minus, z_plus, z_minus, inflow, fringe_ramp):
    grad_x = 0.5 * (x_plus - x_minus)
    grad_y = 0.5 * (y_plus - y_minus)
    grad_z = 0.5 * (z_plus - z_minus)
    gradients = (grad_x, grad_y, grad_z)
    strain = jnp.zeros_like(center[:, 0])
    for comp_a in range(3):
        for comp_b in range(3):
            sym_part = 0.5 * (gradients[comp_b][:, comp_a] + gradients[comp_a][:, comp_b])
            strain = strain + sym_part * sym_part
    eddy_visc = (base_visc + smag_coef * jnp.sqrt(2.0 * strain + strain_floor))[:, None]
    advection = (
        center[:, 0:1] * grad_x + center[:, 1:2] * grad_y + center[:, 2:3] * grad_z
    )
    laplace_term = x_plus + x_minus + y_plus + y_minus + z_plus + z_minus - 6.0 * center
    return -advection + eddy_visc * laplace_term + fringe_ramp * (inflow - center)


def ramp_values(fringe_start, x_cells, fringe_len, total_len):
    offset = (x_cells - fringe_start[0] + total_len) % total_len
    inside = offset < fringe_len
    sine_part = jnp.sin((offset.astype(jnp.float32) + 0.5) * (math.pi / fringe_len))
    return jnp.where(inside, fringe_rate * sine_part * sine_part, 0.0)


def trim(field, margin):
    if margin == 0:
        return field
    return field[..., margin:-margin, margin:-margin, :]


def tendency(field, inflow, fringe_ramp):
    padded = jnp.pad(field, ((0, 0), (0, 0), (0, 0), (0, 0), (1, 1)))
    return combine(
        field[:, :, 1:-1, 1:-1, :],
        field[:, :, 2:, 1:-1, :],
        field[:, :, :-2, 1:-1, :],
        field[:, :, 1:-1, 2:, :],
        field[:, :, 1:-1, :-2, :],
        padded[:, :, 1:-1, 1:-1, 2:],
        padded[:, :, 1:-1, 1:-1, :-2],
        inflow,
        fringe_ramp,
    )


def dft_tables(length):
    positions = jnp.arange(length, dtype=jnp.int32)
    phase = (positions[:, None] * positions[None, :] % length).astype(jnp.float32) * (
        2.0 * math.pi / length
    )
    factor = 1.0 / math.sqrt(length)
    return (jnp.cos(phase) * factor, jnp.sin(phase) * factor)


def on_device(velocity, fringe_start):
    own_field = velocity[0]
    cells_x = own_field.shape[1]
    cells_y = own_field.shape[2]
    levels_z = own_field.shape[3]
    tiles_x = lax.axis_size("gx")
    total_x = cells_x * tiles_x
    total_y = cells_y * lax.axis_size("gy")
    fringe_len = min(8 * cells_x, total_x // 2)
    dom_index = lax.axis_index("dom")
    is_farm = dom_index == 1
    partner = lax.ppermute(own_field, "dom", [(0, 1), (1, 0)])
    precursor = jnp.where(is_farm, partner, own_field)
    farm = jnp.where(is_farm, own_field, partner)
    both = jnp.concatenate([precursor, farm], axis=0)
    extended = with_halo_2d(both, HALO).reshape(
        2, 3, cells_x + 2 * HALO, cells_y + 2 * HALO, levels_z
    )
    x_cells = (
        lax.axis_index("gx") * cells_x
        - HALO
        + total_x
        + jnp.arange(cells_x + 2 * HALO, dtype=jnp.int32)
    ) % total_x
    farm_ramp = ramp_values(fringe_start, x_cells, fringe_len, total_x)
    ramp_full = jnp.stack([jnp.zeros_like(farm_ramp), farm_ramp]).reshape(2, 1, -1, 1, 1)
    inflow = extended[0:1]

    def rates_at(field, margin):
        cut = HALO - margin
        ramp_here = ramp_full[:, :, cut:ramp_full.shape[2] - cut]
        return tendency(field, trim(inflow, cut), ramp_here)

    start = extended
    section_one = trim(start, 1) + time_step * rates_at(start, HALO - 1)
    section_two = 0.75 * trim(start, 2) + 0.25 * (
        trim(section_one, 1) + time_step * rates_at(section_one, HALO - 2)
    )
    section_three = 1.0 / 3.0 * trim(start, 3) + 2.0 / 3.0 * (
        trim(section_two, 1) + time_step * rates_at(section_two, HALO - 3)
    )
    field_out = jnp.where(is_farm, trim(section_three[1], 1), trim(section_three[0], 1))
    beside_all = section_three[1]
    padded = jnp.pad(beside_all[2], ((0, 0), (0, 0), (1, 1)))
    divergence = (
        0.5 * (beside_all[0][2:, 1:-1] - beside_all[0][:-2, 1:-1])
        + 0.5 * (beside_all[1][1:-1, 2:] - beside_all[1][1:-1, :-2])
        + 0.5 * (padded[1:-1, 1:-1, 2:] - padded[1:-1, 1:-1, :-2])
    )
    levels_out = levels_z // (2 * tiles_x)
    tile_block = divergence.reshape(cells_x, cells_y, 2, tiles_x, levels_out)
    own_half = lax.dynamic_index_in_dim(tile_block, dom_index, axis=2, keepdims=False)
    highest = lax.Precision.HIGHEST
    cos_table_x, sin_table_x = dft_tables(total_x)
    cos_table_y, sin_table_y = dft_tables(total_y)
    shard_piece = lax.all_to_all(own_half, "gx", split_axis=2, concat_axis=0, tiled=True)
    real_part = jnp.einsum("xygc,xk->ygck", shard_piece, cos_table_x, precision=highest)
    imag_part = -jnp.einsum("xygc,xk->ygck", shard_piece, sin_table_x, precision=highest)
    parts = jnp.stack([real_part, imag_part])
    parts_in = lax.all_to_all(parts, "gy", split_axis=4, concat_axis=1, tiled=True)
    real_in = parts_in[0]
    imag_in = parts_in[1]
    real_out = jnp.einsum("ygck,yj->gckj", real_in, cos_table_y, precision=highest) + jnp.einsum(
        "ygck,yj->gckj", imag_in, sin_table_y, precision=highest
    )
    imag_out = jnp.einsum("ygck,yj->gckj", imag_in, cos_table_y, precision=highest) - jnp.einsum(
        "ygck,yj->gckj", real_in, sin_table_y, precision=highest
    )
    spectrum = jnp.concatenate([real_out, imag_out])
    return (field_out[None], spectrum)


def solution(mesh):
    in_specs = (P("dom", None, "gx", "gy", None), P())
    out_specs = (P("dom", None, "gx", "gy", None), P(None, ("dom", "gx"), "gy", None))
    return jax.shard_map(
        on_device, mesh=mesh, in_specs=in_specs, out_specs=out_specs, check_vma=False
    )
```

```python
import math

import jax
import jax.numpy as jnp
from jax import lax
from jax.sharding import PartitionSpec as P

time_step = 0.1
fringe_rate = 1.0
smag_coef = 0.03
base_visc = 0.02
strain_floor = 0.25

HALO = 4


def ring_pairs(count, step):
    return [(i, (i + step) % count) for i in range(count)]


def with_halo(block, dim, axis, width):
    count = lax.axis_size(axis)
    size = block.shape[dim]
    low = lax.ppermute(
        lax.slice_in_dim(block, size - width, size, axis=dim), axis, ring_pairs(count, 1)
    )
    high = lax.ppermute(lax.slice_in_dim(block, 0, width, axis=dim), axis, ring_pairs(count, -1))
    return jnp.concatenate([low, block, high], axis=dim)


def with_halo_2d(block, width):
    return with_halo(with_halo(block, 1, "gx", width), 2, "gy", width)


def combine(center, x_plus, x_minus, y_plus, y_minus, z_plus, z_minus, inflow, fringe_ramp):
    grad_x = 0.5 * (x_plus - x_minus)
    grad_y = 0.5 * (y_plus - y_minus)
    grad_z = 0.5 * (z_plus - z_minus)
    gradients = (grad_x, grad_y, grad_z)
    strain = jnp.zeros_like(center[:, 0])
    for comp_a in range(3):
        for comp_b in range(3):
            sym_part = 0.5 * (gradients[comp_b][:, comp_a] + gradients[comp_a][:, comp_b])
            strain = strain + sym_part * sym_part
    eddy_visc = (base_visc + smag_coef * jnp.sqrt(2.0 * strain + strain_floor))[:, None]
    advection = (
        center[:, 0:1] * grad_x + center[:, 1:2] * grad_y + center[:, 2:3] * grad_z
    )
    laplace_term = x_plus + x_minus + y_plus + y_minus + z_plus + z_minus - 6.0 * center
    return -advection + eddy_visc * laplace_term + fringe_ramp * (inflow - center)


def ramp_values(fringe_start, x_cells, fringe_len, total_len):
    offset = (x_cells - fringe_start[0] + total_len) % total_len
    inside = offset < fringe_len
    sine_part = jnp.sin((offset.astype(jnp.float32) + 0.5) * (math.pi / fringe_len))
    return jnp.where(inside, fringe_rate * sine_part * sine_part, 0.0)


def trim(field, margin):
    if margin == 0:
        return field
    return field[..., margin:-margin, margin:-margin, :]


def tendency(field, inflow, fringe_ramp):
    padded = jnp.pad(field, ((0, 0), (0, 0), (0, 0), (0, 0), (1, 1)))
    return combine(
        field[:, :, 1:-1, 1:-1, :],
        field[:, :, 2:, 1:-1, :],
        field[:, :, :-2, 1:-1, :],
        field[:, :, 1:-1, 2:, :],
        field[:, :, 1:-1, :-2, :],
        padded[:, :, 1:-1, 1:-1, 2:],
        padded[:, :, 1:-1, 1:-1, :-2],
        inflow,
        fringe_ramp,
    )


def dft_tables(length):
    positions = jnp.arange(length, dtype=jnp.int32)
    phase = (positions[:, None] * positions[None, :] % length).astype(jnp.float32) * (
        2.0 * math.pi / length
    )
    factor = 1.0 / math.sqrt(length)
    return (jnp.cos(phase) * factor, jnp.sin(phase) * factor)


def on_device(velocity, fringe_start):
    own_field = velocity[0]
    cells_x = own_field.shape[1]
    cells_y = own_field.shape[2]
    levels_z = own_field.shape[3]
    tiles_x = lax.axis_size("gx")
    total_x = cells_x * tiles_x
    total_y = cells_y * lax.axis_size("gy")
    fringe_len = min(8 * cells_x, total_x // 2)
    dom_index = lax.axis_index("dom")
    is_farm = dom_index == 1
    partner = lax.ppermute(own_field, "dom", [(0, 1), (1, 0)])
    precursor = jnp.where(is_farm, partner, own_field)
    farm = jnp.where(is_farm, own_field, partner)
    both = jnp.concatenate([precursor, farm], axis=0)
    extended = with_halo_2d(both, HALO).reshape(
        2, 3, cells_x + 2 * HALO, cells_y + 2 * HALO, levels_z
    )
    x_cells = (
        lax.axis_index("gx") * cells_x
        - HALO
        + total_x
        + jnp.arange(cells_x + 2 * HALO, dtype=jnp.int32)
    ) % total_x
    farm_ramp = ramp_values(fringe_start, x_cells, fringe_len, total_x)
    ramp_full = jnp.stack([jnp.zeros_like(farm_ramp), farm_ramp]).reshape(2, 1, -1, 1, 1)
    inflow = extended[0:1]

    def rates_at(field, margin):
        cut = HALO - margin
        ramp_here = ramp_full[:, :, cut:ramp_full.shape[2] - cut]
        return tendency(field, trim(inflow, cut), ramp_here)

    start = extended
    section_one = trim(start, 1) + time_step * rates_at(start, HALO - 1)
    section_two = 0.75 * trim(start, 2) + 0.25 * (
        trim(section_one, 1) + time_step * rates_at(section_one, HALO - 2)
    )
    section_three = 1.0 / 3.0 * trim(start, 3) + 2.0 / 3.0 * (
        trim(section_two, 1) + time_step * rates_at(section_two, HALO - 3)
    )
    field_out = jnp.where(is_farm, trim(section_three[1], 1), trim(section_three[0], 1))
    beside_all = section_three[1]
    padded = jnp.pad(beside_all[2], ((0, 0), (0, 0), (1, 1)))
    divergence = (
        0.5 * (beside_all[0][2:, 1:-1] - beside_all[0][:-2, 1:-1])
        + 0.5 * (beside_all[1][1:-1, 2:] - beside_all[1][1:-1, :-2])
        + 0.5 * (padded[1:-1, 1:-1, 2:] - padded[1:-1, 1:-1, :-2])
    )
    levels_out = levels_z // (2 * tiles_x)
    tile_block = divergence.reshape(cells_x, cells_y, 2, tiles_x, levels_out)
    own_half = lax.dynamic_index_in_dim(tile_block, dom_index, axis=2, keepdims=False)
    highest = lax.Precision.HIGHEST
    tiles_y = lax.axis_size("gy")
    cos_table_x, sin_table_x = dft_tables(total_x)
    cos_table_y, sin_table_y = dft_tables(total_y)
    table_x = jnp.concatenate([cos_table_x, -sin_table_x], axis=1)
    table_y = jnp.concatenate(
        [
            jnp.concatenate([cos_table_y, -sin_table_y], axis=1),
            jnp.concatenate([sin_table_y, cos_table_y], axis=1),
        ],
        axis=0,
    )
    shard_piece = lax.all_to_all(own_half, "gx", split_axis=2, concat_axis=0, tiled=True)
    lines_x = shard_piece.reshape(total_x, cells_y * levels_out)
    along_x = jnp.dot(lines_x.T, table_x, precision=highest)
    blocks_k = total_x // tiles_y
    along_x = along_x.reshape(cells_y, levels_out, 2, tiles_y, blocks_k)
    parts_in = lax.all_to_all(along_x, "gy", split_axis=3, concat_axis=0, tiled=True)
    lines_y = jnp.transpose(parts_in[:, :, :, 0, :], (1, 3, 2, 0)).reshape(
        levels_out * blocks_k, 2 * total_y
    )
    along_y = jnp.dot(lines_y, table_y, precision=highest)
    spectrum = jnp.transpose(
        along_y.reshape(levels_out, blocks_k, 2, total_y), (2, 0, 1, 3)
    )
    return (field_out[None], spectrum)


def solution(mesh):
    in_specs = (P("dom", None, "gx", "gy", None), P())
    out_specs = (P("dom", None, "gx", "gy", None), P(None, ("dom", "gx"), "gy", None))
    return jax.shard_map(
        on_device, mesh=mesh, in_specs=in_specs, out_specs=out_specs, check_vma=False
    )
```

```python
import math

import jax
import jax.numpy as jnp
from jax import lax
from jax.sharding import PartitionSpec as P

time_step = 0.1
fringe_rate = 1.0
smag_coef = 0.03
base_visc = 0.02
strain_floor = 0.25

HALO = 4


def ring_pairs(count, step):
    return [(i, (i + step) % count) for i in range(count)]


def with_halo(block, dim, axis, width):
    count = lax.axis_size(axis)
    size = block.shape[dim]
    low = lax.ppermute(
        lax.slice_in_dim(block, size - width, size, axis=dim), axis, ring_pairs(count, 1)
    )
    high = lax.ppermute(lax.slice_in_dim(block, 0, width, axis=dim), axis, ring_pairs(count, -1))
    return jnp.concatenate([low, block, high], axis=dim)


def with_halo_2d(block, width):
    return with_halo(with_halo(block, 1, "gx", width), 2, "gy", width)


def combine(center, x_plus, x_minus, y_plus, y_minus, z_plus, z_minus, inflow, fringe_ramp):
    grad_x = 0.5 * (x_plus - x_minus)
    grad_y = 0.5 * (y_plus - y_minus)
    grad_z = 0.5 * (z_plus - z_minus)
    gradients = (grad_x, grad_y, grad_z)
    strain = jnp.zeros_like(center[:, 0])
    for comp_a in range(3):
        for comp_b in range(3):
            sym_part = 0.5 * (gradients[comp_b][:, comp_a] + gradients[comp_a][:, comp_b])
            strain = strain + sym_part * sym_part
    eddy_visc = (base_visc + smag_coef * jnp.sqrt(2.0 * strain + strain_floor))[:, None]
    advection = (
        center[:, 0:1] * grad_x + center[:, 1:2] * grad_y + center[:, 2:3] * grad_z
    )
    laplace_term = x_plus + x_minus + y_plus + y_minus + z_plus + z_minus - 6.0 * center
    return -advection + eddy_visc * laplace_term + fringe_ramp * (inflow - center)


def ramp_values(fringe_start, x_cells, fringe_len, total_len):
    offset = (x_cells - fringe_start[0] + total_len) % total_len
    inside = offset < fringe_len
    sine_part = jnp.sin((offset.astype(jnp.float32) + 0.5) * (math.pi / fringe_len))
    return jnp.where(inside, fringe_rate * sine_part * sine_part, 0.0)


def trim(field, margin):
    if margin == 0:
        return field
    return field[..., margin:-margin, margin:-margin, :]


def tendency(field, inflow, fringe_ramp):
    padded = jnp.pad(field, ((0, 0), (0, 0), (0, 0), (0, 0), (1, 1)))
    return combine(
        field[:, :, 1:-1, 1:-1, :],
        field[:, :, 2:, 1:-1, :],
        field[:, :, :-2, 1:-1, :],
        field[:, :, 1:-1, 2:, :],
        field[:, :, 1:-1, :-2, :],
        padded[:, :, 1:-1, 1:-1, 2:],
        padded[:, :, 1:-1, 1:-1, :-2],
        inflow,
        fringe_ramp,
    )


def dft_tables(length):
    positions = jnp.arange(length, dtype=jnp.int32)
    phase = (positions[:, None] * positions[None, :] % length).astype(jnp.float32) * (
        2.0 * math.pi / length
    )
    factor = 1.0 / math.sqrt(length)
    return (jnp.cos(phase) * factor, jnp.sin(phase) * factor)


def stacked_dft_x(length, inner):
    outer = length // inner
    k = jnp.arange(length, dtype=jnp.int32)[:, None]
    a = jnp.arange(outer, dtype=jnp.int32)[None, :]
    b = jnp.arange(inner, dtype=jnp.int32)[None, :]
    step = 2.0 * math.pi / length
    phase_a = ((inner * a * k) % length).astype(jnp.float32) * step
    phase_b = ((b * k) % length).astype(jnp.float32) * step
    factor = 1.0 / math.sqrt(length)
    cos_a = (jnp.cos(phase_a) * factor)[:, :, None]
    sin_a = (jnp.sin(phase_a) * factor)[:, :, None]
    cos_b = jnp.cos(phase_b)[:, None, :]
    sin_b = jnp.sin(phase_b)[:, None, :]
    real = (cos_a * cos_b - sin_a * sin_b).reshape(length, length)
    imag = -(cos_a * sin_b + sin_a * cos_b).reshape(length, length)
    return jnp.concatenate([real, imag], axis=0)


def on_device(velocity, fringe_start):
    own_field = velocity[0]
    cells_x = own_field.shape[1]
    cells_y = own_field.shape[2]
    levels_z = own_field.shape[3]
    tiles_x = lax.axis_size("gx")
    total_x = cells_x * tiles_x
    total_y = cells_y * lax.axis_size("gy")
    fringe_len = min(8 * cells_x, total_x // 2)
    dom_index = lax.axis_index("dom")
    is_farm = dom_index == 1
    partner = lax.ppermute(own_field, "dom", [(0, 1), (1, 0)])
    precursor = jnp.where(is_farm, partner, own_field)
    farm = jnp.where(is_farm, own_field, partner)
    both = jnp.concatenate([precursor, farm], axis=0)
    extended = with_halo_2d(both, HALO).reshape(
        2, 3, cells_x + 2 * HALO, cells_y + 2 * HALO, levels_z
    )
    x_cells = (
        lax.axis_index("gx") * cells_x
        - HALO
        + total_x
        + jnp.arange(cells_x + 2 * HALO, dtype=jnp.int32)
    ) % total_x
    farm_ramp = ramp_values(fringe_start, x_cells, fringe_len, total_x)
    ramp_full = jnp.stack([jnp.zeros_like(farm_ramp), farm_ramp]).reshape(2, 1, -1, 1, 1)
    inflow = extended[0:1]

    def rates_at(field, margin):
        cut = HALO - margin
        ramp_here = ramp_full[:, :, cut:ramp_full.shape[2] - cut]
        return tendency(field, trim(inflow, cut), ramp_here)

    start = extended
    section_one = trim(start, 1) + time_step * rates_at(start, HALO - 1)
    section_two = 0.75 * trim(start, 2) + 0.25 * (
        trim(section_one, 1) + time_step * rates_at(section_one, HALO - 2)
    )
    section_three = 1.0 / 3.0 * trim(start, 3) + 2.0 / 3.0 * (
        trim(section_two, 1) + time_step * rates_at(section_two, HALO - 3)
    )
    field_out = jnp.where(is_farm, trim(section_three[1], 1), trim(section_three[0], 1))
    beside_all = section_three[1]
    padded = jnp.pad(beside_all[2], ((0, 0), (0, 0), (1, 1)))
    divergence = (
        0.5 * (beside_all[0][2:, 1:-1] - beside_all[0][:-2, 1:-1])
        + 0.5 * (beside_all[1][1:-1, 2:] - beside_all[1][1:-1, :-2])
        + 0.5 * (padded[1:-1, 1:-1, 2:] - padded[1:-1, 1:-1, :-2])
    )
    levels_out = levels_z // (2 * tiles_x)
    tile_block = divergence.reshape(cells_x, cells_y, 2, tiles_x, levels_out)
    own_half = lax.dynamic_index_in_dim(tile_block, dom_index, axis=2, keepdims=False)
    highest = lax.Precision.HIGHEST
    tiles_y = lax.axis_size("gy")
    table_x = stacked_dft_x(total_x, cells_x)
    cos_table_y, sin_table_y = dft_tables(total_y)
    table_y = jnp.concatenate(
        [
            jnp.concatenate([cos_table_y, sin_table_y], axis=1),
            jnp.concatenate([-sin_table_y, cos_table_y], axis=1),
        ],
        axis=0,
    )
    shard_piece = lax.all_to_all(own_half, "gx", split_axis=2, concat_axis=0, tiled=True)
    lines_x = shard_piece.reshape(total_x, cells_y * levels_out)
    along_x = jnp.dot(table_x, lines_x, precision=highest)
    blocks_k = total_x // tiles_y
    along_x = along_x.reshape(2, tiles_y, blocks_k, cells_y, levels_out)
    parts_in = lax.all_to_all(along_x, "gy", split_axis=1, concat_axis=3, tiled=True)
    lines_y = jnp.transpose(parts_in[:, 0], (0, 2, 3, 1)).reshape(2 * total_y, levels_out * blocks_k)
    along_y = jnp.dot(table_y, lines_y, precision=highest)
    spectrum = jnp.transpose(
        along_y.reshape(2, total_y, levels_out, blocks_k), (0, 2, 3, 1)
    )
    return (field_out[None], spectrum)


def solution(mesh):
    in_specs = (P("dom", None, "gx", "gy", None), P())
    out_specs = (P("dom", None, "gx", "gy", None), P(None, ("dom", "gx"), "gy", None))
    return jax.shard_map(
        on_device, mesh=mesh, in_specs=in_specs, out_specs=out_specs, check_vma=False
    )
```

```python
import math

import jax
import jax.numpy as jnp
from jax import lax
from jax.sharding import PartitionSpec as P

time_step = 0.1
fringe_rate = 1.0
smag_coef = 0.03
base_visc = 0.02
strain_floor = 0.25

HALO = 4


def ring_pairs(count, step):
    return [(i, (i + step) % count) for i in range(count)]


def with_halo(block, dim, axis, width):
    count = lax.axis_size(axis)
    size = block.shape[dim]
    low = lax.ppermute(
        lax.slice_in_dim(block, size - width, size, axis=dim), axis, ring_pairs(count, 1)
    )
    high = lax.ppermute(lax.slice_in_dim(block, 0, width, axis=dim), axis, ring_pairs(count, -1))
    return jnp.concatenate([low, block, high], axis=dim)


def with_halo_2d(block, width):
    return with_halo(with_halo(block, 1, "gx", width), 2, "gy", width)


def combine(center, x_plus, x_minus, y_plus, y_minus, z_plus, z_minus, inflow, fringe_ramp):
    grad_x = 0.5 * (x_plus - x_minus)
    grad_y = 0.5 * (y_plus - y_minus)
    grad_z = 0.5 * (z_plus - z_minus)
    gradients = (grad_x, grad_y, grad_z)
    strain = jnp.zeros_like(center[:, 0])
    for comp_a in range(3):
        for comp_b in range(3):
            sym_part = 0.5 * (gradients[comp_b][:, comp_a] + gradients[comp_a][:, comp_b])
            strain = strain + sym_part * sym_part
    eddy_visc = (base_visc + smag_coef * jnp.sqrt(2.0 * strain + strain_floor))[:, None]
    advection = (
        center[:, 0:1] * grad_x + center[:, 1:2] * grad_y + center[:, 2:3] * grad_z
    )
    laplace_term = x_plus + x_minus + y_plus + y_minus + z_plus + z_minus - 6.0 * center
    return -advection + eddy_visc * laplace_term + fringe_ramp * (inflow - center)


def ramp_values(fringe_start, x_cells, fringe_len, total_len):
    offset = (x_cells - fringe_start[0] + total_len) % total_len
    inside = offset < fringe_len
    sine_part = jnp.sin((offset.astype(jnp.float32) + 0.5) * (math.pi / fringe_len))
    return jnp.where(inside, fringe_rate * sine_part * sine_part, 0.0)


def trim(field, margin):
    if margin == 0:
        return field
    return field[..., margin:-margin, margin:-margin, :]


def tendency(field, inflow, fringe_ramp):
    padded = jnp.pad(field, ((0, 0), (0, 0), (0, 0), (0, 0), (1, 1)))
    return combine(
        field[:, :, 1:-1, 1:-1, :],
        field[:, :, 2:, 1:-1, :],
        field[:, :, :-2, 1:-1, :],
        field[:, :, 1:-1, 2:, :],
        field[:, :, 1:-1, :-2, :],
        padded[:, :, 1:-1, 1:-1, 2:],
        padded[:, :, 1:-1, 1:-1, :-2],
        inflow,
        fringe_ramp,
    )


def dft_tables(length):
    positions = jnp.arange(length, dtype=jnp.int32)
    phase = (positions[:, None] * positions[None, :] % length).astype(jnp.float32) * (
        2.0 * math.pi / length
    )
    factor = 1.0 / math.sqrt(length)
    return (jnp.cos(phase) * factor, jnp.sin(phase) * factor)


def stacked_dft_x(length, inner):
    outer = length // inner
    k = jnp.arange(length, dtype=jnp.int32)[:, None]
    a = jnp.arange(outer, dtype=jnp.int32)[None, :]
    b = jnp.arange(inner, dtype=jnp.int32)[None, :]
    step = 2.0 * math.pi / length
    phase_a = ((inner * a * k) % length).astype(jnp.float32) * step
    phase_b = ((b * k) % length).astype(jnp.float32) * step
    factor = 1.0 / math.sqrt(length)
    cos_a = (jnp.cos(phase_a) * factor)[:, :, None]
    sin_a = (jnp.sin(phase_a) * factor)[:, :, None]
    cos_b = jnp.cos(phase_b)[:, None, :]
    sin_b = jnp.sin(phase_b)[:, None, :]
    real = (cos_a * cos_b - sin_a * sin_b).reshape(length, length)
    imag = -(cos_a * sin_b + sin_a * cos_b).reshape(length, length)
    return jnp.concatenate([real, imag], axis=0)


def on_device(velocity, fringe_start):
    own_field = velocity[0]
    cells_x = own_field.shape[1]
    cells_y = own_field.shape[2]
    levels_z = own_field.shape[3]
    tiles_x = lax.axis_size("gx")
    total_x = cells_x * tiles_x
    total_y = cells_y * lax.axis_size("gy")
    fringe_len = min(8 * cells_x, total_x // 2)
    dom_index = lax.axis_index("dom")
    is_farm = dom_index == 1
    partner = lax.ppermute(own_field, "dom", [(0, 1), (1, 0)])
    precursor = jnp.where(is_farm, partner, own_field)
    farm = jnp.where(is_farm, own_field, partner)
    both = jnp.concatenate([precursor, farm], axis=0)
    extended = with_halo_2d(both, HALO).reshape(
        2, 3, cells_x + 2 * HALO, cells_y + 2 * HALO, levels_z
    )
    x_cells = (
        lax.axis_index("gx") * cells_x
        - HALO
        + total_x
        + jnp.arange(cells_x + 2 * HALO, dtype=jnp.int32)
    ) % total_x
    farm_ramp = ramp_values(fringe_start, x_cells, fringe_len, total_x)
    ramp_full = jnp.stack([jnp.zeros_like(farm_ramp), farm_ramp]).reshape(2, 1, -1, 1, 1)
    inflow = extended[0:1]

    def rates_at(field, margin):
        cut = HALO - margin
        ramp_here = ramp_full[:, :, cut:ramp_full.shape[2] - cut]
        return tendency(field, trim(inflow, cut), ramp_here)

    start = extended
    section_one = trim(start, 1) + time_step * rates_at(start, HALO - 1)
    section_two = 0.75 * trim(start, 2) + 0.25 * (
        trim(section_one, 1) + time_step * rates_at(section_one, HALO - 2)
    )
    section_three = 1.0 / 3.0 * trim(start, 3) + 2.0 / 3.0 * (
        trim(section_two, 1) + time_step * rates_at(section_two, HALO - 3)
    )
    field_out = jnp.where(is_farm, trim(section_three[1], 1), trim(section_three[0], 1))
    beside_all = section_three[1]
    padded = jnp.pad(beside_all[2], ((0, 0), (0, 0), (1, 1)))
    divergence = (
        0.5 * (beside_all[0][2:, 1:-1] - beside_all[0][:-2, 1:-1])
        + 0.5 * (beside_all[1][1:-1, 2:] - beside_all[1][1:-1, :-2])
        + 0.5 * (padded[1:-1, 1:-1, 2:] - padded[1:-1, 1:-1, :-2])
    )
    levels_out = levels_z // (2 * tiles_x)
    tile_block = divergence.reshape(cells_x, cells_y, 2, tiles_x, levels_out)
    own_half = lax.dynamic_index_in_dim(tile_block, dom_index, axis=2, keepdims=False)
    highest = lax.Precision.HIGH
    tiles_y = lax.axis_size("gy")
    table_x = stacked_dft_x(total_x, cells_x)
    cos_table_y, sin_table_y = dft_tables(total_y)
    table_y = jnp.concatenate(
        [
            jnp.concatenate([cos_table_y, sin_table_y], axis=1),
            jnp.concatenate([-sin_table_y, cos_table_y], axis=1),
        ],
        axis=0,
    )
    shard_piece = lax.all_to_all(own_half, "gx", split_axis=2, concat_axis=0, tiled=True)
    lines_x = shard_piece.reshape(total_x, cells_y * levels_out)
    along_x = jnp.dot(table_x, lines_x, precision=highest)
    blocks_k = total_x // tiles_y
    along_x = along_x.reshape(2, tiles_y, blocks_k, cells_y, levels_out)
    parts_in = lax.all_to_all(along_x, "gy", split_axis=1, concat_axis=3, tiled=True)
    lines_y = jnp.transpose(parts_in[:, 0], (0, 2, 3, 1)).reshape(2 * total_y, levels_out * blocks_k)
    along_y = jnp.dot(table_y, lines_y, precision=highest)
    spectrum = jnp.transpose(
        along_y.reshape(2, total_y, levels_out, blocks_k), (0, 2, 3, 1)
    )
    return (field_out[None], spectrum)


def solution(mesh):
    in_specs = (P("dom", None, "gx", "gy", None), P())
    out_specs = (P("dom", None, "gx", "gy", None), P(None, ("dom", "gx"), "gy", None))
    return jax.shard_map(
        on_device, mesh=mesh, in_specs=in_specs, out_specs=out_specs, check_vma=False
    )
```

```python
import math

import jax
import jax.numpy as jnp
from jax import lax
from jax.sharding import PartitionSpec as P

time_step = 0.1
fringe_rate = 1.0
smag_coef = 0.03
base_visc = 0.02
strain_floor = 0.25

HALO = 4


def ring_pairs(count, step):
    return [(i, (i + step) % count) for i in range(count)]


def with_halo(block, dim, axis, width):
    count = lax.axis_size(axis)
    size = block.shape[dim]
    first = lax.slice_in_dim(block, 0, width, axis=dim)
    last = lax.slice_in_dim(block, size - width, size, axis=dim)
    odd = lax.axis_index(axis) % 2 == 1
    inner_pairs = [(i, i ^ 1) for i in range(count)]
    outer_pairs = [(i, (i + 1) % count if i % 2 else (i - 1) % count) for i in range(count)]
    inner = lax.ppermute(jnp.where(odd, first, last), axis, inner_pairs)
    outer = lax.ppermute(jnp.where(odd, last, first), axis, outer_pairs)
    low = jnp.where(odd, inner, outer)
    high = jnp.where(odd, outer, inner)
    return jnp.concatenate([low, block, high], axis=dim)


def with_halo_2d(block, width):
    return with_halo(with_halo(block, 1, "gx", width), 2, "gy", width)


def combine(center, x_plus, x_minus, y_plus, y_minus, z_plus, z_minus, inflow, fringe_ramp):
    grad_x = 0.5 * (x_plus - x_minus)
    grad_y = 0.5 * (y_plus - y_minus)
    grad_z = 0.5 * (z_plus - z_minus)
    gradients = (grad_x, grad_y, grad_z)
    strain = jnp.zeros_like(center[:, 0])
    for comp_a in range(3):
        for comp_b in range(3):
            sym_part = 0.5 * (gradients[comp_b][:, comp_a] + gradients[comp_a][:, comp_b])
            strain = strain + sym_part * sym_part
    eddy_visc = (base_visc + smag_coef * jnp.sqrt(2.0 * strain + strain_floor))[:, None]
    advection = (
        center[:, 0:1] * grad_x + center[:, 1:2] * grad_y + center[:, 2:3] * grad_z
    )
    laplace_term = x_plus + x_minus + y_plus + y_minus + z_plus + z_minus - 6.0 * center
    return -advection + eddy_visc * laplace_term + fringe_ramp * (inflow - center)


def ramp_values(fringe_start, x_cells, fringe_len, total_len):
    offset = (x_cells - fringe_start[0] + total_len) % total_len
    inside = offset < fringe_len
    sine_part = jnp.sin((offset.astype(jnp.float32) + 0.5) * (math.pi / fringe_len))
    return jnp.where(inside, fringe_rate * sine_part * sine_part, 0.0)


def trim(field, margin):
    if margin == 0:
        return field
    return field[..., margin:-margin, margin:-margin, :]


def tendency(field, inflow, fringe_ramp):
    padded = jnp.pad(field, ((0, 0), (0, 0), (0, 0), (0, 0), (1, 1)))
    return combine(
        field[:, :, 1:-1, 1:-1, :],
        field[:, :, 2:, 1:-1, :],
        field[:, :, :-2, 1:-1, :],
        field[:, :, 1:-1, 2:, :],
        field[:, :, 1:-1, :-2, :],
        padded[:, :, 1:-1, 1:-1, 2:],
        padded[:, :, 1:-1, 1:-1, :-2],
        inflow,
        fringe_ramp,
    )


def dft_tables(length):
    positions = jnp.arange(length, dtype=jnp.int32)
    phase = (positions[:, None] * positions[None, :] % length).astype(jnp.float32) * (
        2.0 * math.pi / length
    )
    factor = 1.0 / math.sqrt(length)
    return (jnp.cos(phase) * factor, jnp.sin(phase) * factor)


def stacked_dft_x(length, inner):
    outer = length // inner
    k = jnp.arange(length, dtype=jnp.int32)[:, None]
    a = jnp.arange(outer, dtype=jnp.int32)[None, :]
    b = jnp.arange(inner, dtype=jnp.int32)[None, :]
    step = 2.0 * math.pi / length
    phase_a = ((inner * a * k) % length).astype(jnp.float32) * step
    phase_b = ((b * k) % length).astype(jnp.float32) * step
    factor = 1.0 / math.sqrt(length)
    cos_a = (jnp.cos(phase_a) * factor)[:, :, None]
    sin_a = (jnp.sin(phase_a) * factor)[:, :, None]
    cos_b = jnp.cos(phase_b)[:, None, :]
    sin_b = jnp.sin(phase_b)[:, None, :]
    real = (cos_a * cos_b - sin_a * sin_b).reshape(length, length)
    imag = -(cos_a * sin_b + sin_a * cos_b).reshape(length, length)
    return jnp.concatenate([real, imag], axis=0)


def on_device(velocity, fringe_start):
    own_field = velocity[0]
    cells_x = own_field.shape[1]
    cells_y = own_field.shape[2]
    levels_z = own_field.shape[3]
    tiles_x = lax.axis_size("gx")
    total_x = cells_x * tiles_x
    total_y = cells_y * lax.axis_size("gy")
    fringe_len = min(8 * cells_x, total_x // 2)
    dom_index = lax.axis_index("dom")
    is_farm = dom_index == 1
    partner = lax.ppermute(own_field, "dom", [(0, 1), (1, 0)])
    precursor = jnp.where(is_farm, partner, own_field)
    farm = jnp.where(is_farm, own_field, partner)
    both = jnp.concatenate([precursor, farm], axis=0)
    extended = with_halo_2d(both, HALO).reshape(
        2, 3, cells_x + 2 * HALO, cells_y + 2 * HALO, levels_z
    )
    x_cells = (
        lax.axis_index("gx") * cells_x
        - HALO
        + total_x
        + jnp.arange(cells_x + 2 * HALO, dtype=jnp.int32)
    ) % total_x
    farm_ramp = ramp_values(fringe_start, x_cells, fringe_len, total_x)
    ramp_full = jnp.stack([jnp.zeros_like(farm_ramp), farm_ramp]).reshape(2, 1, -1, 1, 1)
    inflow = extended[0:1]

    def rates_at(field, margin):
        cut = HALO - margin
        ramp_here = ramp_full[:, :, cut:ramp_full.shape[2] - cut]
        return tendency(field, trim(inflow, cut), ramp_here)

    start = extended
    section_one = trim(start, 1) + time_step * rates_at(start, HALO - 1)
    section_two = 0.75 * trim(start, 2) + 0.25 * (
        trim(section_one, 1) + time_step * rates_at(section_one, HALO - 2)
    )
    section_three = 1.0 / 3.0 * trim(start, 3) + 2.0 / 3.0 * (
        trim(section_two, 1) + time_step * rates_at(section_two, HALO - 3)
    )
    field_out = jnp.where(is_farm, trim(section_three[1], 1), trim(section_three[0], 1))
    beside_all = section_three[1]
    padded = jnp.pad(beside_all[2], ((0, 0), (0, 0), (1, 1)))
    divergence = (
        0.5 * (beside_all[0][2:, 1:-1] - beside_all[0][:-2, 1:-1])
        + 0.5 * (beside_all[1][1:-1, 2:] - beside_all[1][1:-1, :-2])
        + 0.5 * (padded[1:-1, 1:-1, 2:] - padded[1:-1, 1:-1, :-2])
    )
    levels_out = levels_z // (2 * tiles_x)
    tile_block = divergence.reshape(cells_x, cells_y, 2, tiles_x, levels_out)
    own_half = lax.dynamic_index_in_dim(tile_block, dom_index, axis=2, keepdims=False)
    highest = lax.Precision.HIGH
    tiles_y = lax.axis_size("gy")
    table_x = stacked_dft_x(total_x, cells_x)
    cos_table_y, sin_table_y = dft_tables(total_y)
    table_y = jnp.concatenate(
        [
            jnp.concatenate([cos_table_y, sin_table_y], axis=1),
            jnp.concatenate([-sin_table_y, cos_table_y], axis=1),
        ],
        axis=0,
    )
    shard_piece = lax.all_to_all(own_half, "gx", split_axis=2, concat_axis=0, tiled=True)
    lines_x = shard_piece.reshape(total_x, cells_y * levels_out)
    along_x = jnp.dot(table_x, lines_x, precision=highest)
    blocks_k = total_x // tiles_y
    along_x = along_x.reshape(2, tiles_y, blocks_k, cells_y, levels_out)
    parts_in = lax.all_to_all(along_x, "gy", split_axis=1, concat_axis=3, tiled=True)
    lines_y = jnp.transpose(parts_in[:, 0], (0, 2, 3, 1)).reshape(2 * total_y, levels_out * blocks_k)
    along_y = jnp.dot(table_y, lines_y, precision=highest)
    spectrum = jnp.transpose(
        along_y.reshape(2, total_y, levels_out, blocks_k), (0, 2, 3, 1)
    )
    return (field_out[None], spectrum)


def solution(mesh):
    in_specs = (P("dom", None, "gx", "gy", None), P())
    out_specs = (P("dom", None, "gx", "gy", None), P(None, ("dom", "gx"), "gy", None))
    return jax.shard_map(
        on_device, mesh=mesh, in_specs=in_specs, out_specs=out_specs, check_vma=False
    )
```
